512 devices in a mesh: band: 8 (over x_lo, y), xy: 64 (over z, x_hi, core).
Axes of the slice: x: 4 (x_hi: 2, x_lo: 2; x = x_hi * 2 + x_lo), y: 4, z: 16, core: 2. Of those that a mesh axis runs over, the one named last changes fastest.
Arguments:
- orbitals: float32 [16, 64, 128, 256], P('band', 'xy'), may hold values from -6 to 6
- energies: float32 [16], P('band'), may hold values from -1.5 to -0.25
- occupation: int32 [16], P('band'), may hold values from 1 to 2
- potential: float32 [64, 128, 256], P('xy'), may hold values from 0.25 to 2
- trials: float32 [4, 64, 128, 256], P(None, 'xy'), may hold values from -8 to 23
Outputs:
- density: float32 [4, 64, 128, 256], P(None, 'xy', 'band')
- response_matrix: float32 [4, 4], replicated
The draws below stay inside these ranges and needn't reach their ends.
All inputs are finite; a program needn't handle non-finite values.
Results may differ from the reference program's by a relative error of at most 0.0001.
Values sent between devices are 32-bit elements; how exact they have to be, the bound alone decides.
No kernel may reach another device: no remote copies, remote signals or barrier semaphores. Data moves between devices by JAX's collectives and lax.ppermute only.
A program may use at most 64 MiB of HBM per device.

```python
import math
import jax
import jax.numpy as jnp
from jax import lax

NY = 128
NZ = 256
K = 4
ITERS = 3
NX = 64
NB = 16


def cosine_rows(frequency, offsets, length):
    positions = jnp.arange(length, dtype=jnp.int32)
    reduced = frequency[..., None] * positions % length
    return jnp.cos(2.0 * math.pi / length * reduced.astype(jnp.float32) + offsets[..., None])


def draw_orbitals(key, part):
    ordering = jax.random.permutation(jax.random.fold_in(key, 3), 64)[:NB]
    freq_x = 1 + ordering % 4
    freq_y = 1 + ordering // 4 % 4
    freq_z = 1 + ordering // 16
    offsets = jax.random.uniform(jax.random.fold_in(key, 5), (3, NB), jnp.float32, 0.0, 2.0 * math.pi)
    along_x = cosine_rows(freq_x, offsets[0], NX)
    along_y = cosine_rows(freq_y, offsets[1], NY)
    along_z = cosine_rows(freq_z, offsets[2], NZ)
    modes = math.sqrt(8.0) * along_x[:, :, None, None] * along_y[:, None, :, None] * along_z[:, None, None, :]
    noise_key = jax.random.fold_in(key, 11)
    noise = 0.5 * jnp.clip(jax.random.normal(noise_key, (NB, NX, NY, NZ), jnp.float32), -6.0, 6.0)
    return (modes + noise).astype(jnp.float32)


def draw_trials(key, part):
    amplitude = 0.4
    frequency = jnp.broadcast_to(jnp.arange(1, 5, dtype=jnp.int32), (K, 4))

    def smooth_factor(index, length):
        weights = jax.random.uniform(jax.random.fold_in(key, 20 + index), (K, 4), jnp.float32, -amplitude, amplitude)
        offsets = jax.random.uniform(jax.random.fold_in(key, 30 + index), (K, 4), jnp.float32, 0.0, 2.0 * math.pi)
        return 1.0 + jnp.sum(weights[:, :, None] * cosine_rows(frequency, offsets, length), axis=1)
    factor_x = smooth_factor(0, NX)
    factor_y = smooth_factor(1, NY)
    factor_z = smooth_factor(2, NZ)
    smooth = factor_x[:, :, None, None] * factor_y[:, None, :, None] * factor_z[:, None, None, :]
    rough_key = jax.random.fold_in(key, 41)
    rough = jax.random.uniform(rough_key, (K, NX, NY, NZ), jnp.float32, -0.5, 0.5)
    return (smooth + rough).astype(jnp.float32)


def place_ends(drawn, own_key, low, largest):
    spot = [jax.random.randint(jax.random.fold_in(own_key, axis), (), 0, length) for axis, length in enumerate(drawn.shape)]
    longest = drawn.shape.index(max(drawn.shape))
    neighbour = spot[:longest] + [(spot[longest] + 1) % drawn.shape[longest]] + spot[longest + 1:]
    return drawn.at[tuple(spot)].set(low).at[tuple(neighbour)].set(largest)


def block_levels(rng, dims, split, low, top_value):
    gain = 1.0
    for dim, shards_of in split:
        steps = jax.random.uniform(jax.random.fold_in(jax.random.fold_in(rng, 6), dim), (shards_of,), jnp.float32, low / len(split), top_value / len(split))
        gain = gain * jnp.repeat(jnp.exp(steps), dims[dim] // shards_of).reshape((-1,) + (1,) * (len(dims) - 1 - dim))
    return gain


def setup_inputs(seed: int = 0) -> dict:
    arg_keys = jax.random.split(jax.random.key(seed), 6)
    orbitals = draw_orbitals(jax.random.fold_in(arg_keys[5], 71), 0)
    energies = jnp.clip(-1.5 + 1.25 * jax.random.uniform(arg_keys[1], (NB,), jnp.float32) ** block_levels(arg_keys[1], (NB,), ((0, 8),), -0.2, 0.2), -1.5, -0.25)
    occupation = place_ends(jax.random.randint(arg_keys[2], (NB,), 1, 3), jax.random.fold_in(arg_keys[2], 1), 1, 2).astype(jnp.int32)
    potential = jnp.clip(0.25 + 1.75 * jax.random.uniform(arg_keys[3], (NX, NY, NZ), jnp.float32) ** block_levels(arg_keys[3], (NX, NY, NZ), ((0, 64),), -0.2, 0.2), 0.25, 2.0)
    trials = draw_trials(jax.random.fold_in(arg_keys[5], 71), 0)
    return dict(orbitals=orbitals, energies=energies, occupation=occupation, potential=potential, trials=trials)


def reference(orbitals, energies, occupation, potential, trials):
    orbital_total = orbitals.shape[0]
    trial_count = trials.shape[0]
    cell_total = potential.size
    grid_shape = potential.shape
    highest = lax.Precision.HIGHEST
    psi_flat = orbitals.reshape(orbital_total, cell_total)
    trial_flat = trials.reshape(trial_count, cell_total)
    potential_flat = potential.reshape(1, cell_total)

    def project(vectors):
        intersection = jnp.dot(psi_flat, vectors.T, precision=highest, preferred_element_type=jnp.float32) / cell_total
        return vectors - jnp.dot(intersection.T, psi_flat, precision=highest, preferred_element_type=jnp.float32)

    def apply_op(vectors, diagonal_op):
        field_block = vectors.reshape((trial_count,) + grid_shape)
        beside = jnp.roll(field_block, 1, 1) + jnp.roll(field_block, -1, 1)
        beside = beside + jnp.roll(field_block, 1, 2) + jnp.roll(field_block, -1, 2)
        z_padded = jnp.pad(field_block, ((0, 0), (0, 0), (0, 0), (1, 1)))
        beside = beside + z_padded[..., 2:] + z_padded[..., :-2]
        return diagonal_op * vectors - 0.5 * beside.reshape(trial_count, cell_total)

    def one_orbital(running, inputs):
        psi_row, energy, weight = inputs
        diagonal_op = 3.0 + potential_flat - energy
        right_side = -project(trial_flat * psi_row[None, :])
        update = project(right_side / diagonal_op)
        for iteration in range(ITERS):
            residual = right_side - apply_op(update, diagonal_op)
            update = update + project(residual / diagonal_op)
        return (running + (weight * psi_row)[None, :] * update, None)
    initial = jnp.zeros((trial_count, cell_total), jnp.float32)
    running, unused = lax.scan(one_orbital, initial, (psi_flat, energies, occupation.astype(jnp.float32)))
    density = running / math.sqrt(orbital_total)
    response_matrix = jnp.dot(density, trial_flat.T, precision=highest, preferred_element_type=jnp.float32) / cell_total
    return (density.reshape((trial_count,) + grid_shape), response_matrix)
```

```python
import math

import jax
import jax.numpy as jnp
from jax import lax
from jax.sharding import PartitionSpec as P

ITERS = 3


def padded_2(block, sides, width):
    for axis, dim in sides:
        count = lax.axis_size(axis)
        forward = [(i, i + 1) for i in range(count - 1)]
        forward.append((count - 1, 0))
        backward = [(target, source) for source, target in forward]
        low = lax.ppermute(
            lax.slice_in_dim(block, block.shape[dim] - width, None, axis=dim), axis, forward
        )
        high = lax.ppermute(lax.slice_in_dim(block, 0, width, axis=dim), axis, backward)
        block = jnp.concatenate([low, block, high], axis=dim)
    return block


def tree_sum(value, axes):
    for axis in axes:
        count = lax.axis_size(axis)
        step = 1
        while step < count:
            pairs = [(i, i ^ step) for i in range(count)]
            value = value + lax.ppermute(value, axis, pairs)
            step *= 2
    return value


def respond(psi_rows, energy_rows, weight_rows, potential_part, trial_part, project, apply_op):
    orbital_count, cell_count = psi_rows.shape
    trial_count = trial_part.shape[0]
    row_count = orbital_count * trial_count
    diagonal_op = 3.0 + potential_part.reshape(1, 1, cell_count) - energy_rows[:, None, None]
    diagonal_op = jnp.broadcast_to(diagonal_op, (orbital_count, trial_count, cell_count)).reshape(
        row_count, cell_count
    )
    products = trial_part[None, :, :] * psi_rows[:, None, :]
    right_side = -project(products.reshape(row_count, cell_count))
    update = project(right_side / diagonal_op)
    for iteration in range(ITERS):
        residual = right_side - apply_op(update, diagonal_op)
        update = update + project(residual / diagonal_op)
    weights = weight_rows[:, None, None] * psi_rows[:, None, :]
    return jnp.sum(weights * update.reshape(orbital_count, trial_count, cell_count), axis=0)


def neighbours_z(field_block):
    z_padded = jnp.pad(field_block, ((0, 0), (0, 0), (0, 0), (1, 1)))
    return z_padded[..., 2:] + z_padded[..., :-2]


def local(orbitals, energies, occupation, potential, trials):
    nb_dev, width_x, width_y, width_z = orbitals.shape
    trial_count = trials.shape[0]
    cell_count = width_x * width_y * width_z
    cell_total = cell_count * lax.axis_size("xy")
    orbital_total = nb_dev * lax.axis_size("band")
    y_share = width_y // lax.axis_size("band")
    band_index = lax.axis_index("band")
    highest = lax.Precision.HIGHEST
    trial_slice = lax.dynamic_slice_in_dim(trials, band_index * y_share, y_share, 2)
    psi_flat = orbitals.reshape(nb_dev, cell_count)
    psi_all = lax.all_gather(psi_flat, "band", axis=0, tiled=True)

    def project_slab(vectors):
        intersection = jnp.dot(
            psi_all, vectors.T, precision=highest, preferred_element_type=jnp.float32
        )
        intersection = tree_sum(intersection, ("xy",)) / cell_total
        return vectors - jnp.dot(
            intersection.T, psi_all, precision=highest, preferred_element_type=jnp.float32
        )

    def apply_slab(vectors, diagonal_op):
        field_block = vectors.reshape(-1, width_x, width_y, width_z)
        padded = padded_2(field_block, (("xy", 1),), 1)
        beside = padded[:, 2:] + padded[:, :-2]
        beside = beside + jnp.roll(field_block, 1, 2) + jnp.roll(field_block, -1, 2)
        beside = beside + neighbours_z(field_block)
        return diagonal_op * vectors - 0.5 * beside.reshape(vectors.shape)

    summed = respond(
        psi_flat,
        energies,
        occupation.astype(jnp.float32),
        potential.reshape(cell_count),
        trials.reshape(trial_count, cell_count),
        project_slab,
        apply_slab,
    )
    partial_grid = (summed / math.sqrt(orbital_total)).reshape(
        trial_count, width_x, width_y, width_z
    )
    density = lax.psum_scatter(partial_grid, "band", scatter_dimension=2, tiled=True)
    local_sum = jnp.dot(
        density.reshape(trial_count, -1),
        trial_slice.reshape(trial_count, -1).T,
        precision=highest,
        preferred_element_type=jnp.float32,
    )
    response_matrix = tree_sum(local_sum, ("band", "xy")) / cell_total
    return (density, response_matrix)


def solution(mesh):
    in_specs = (
        P("band", "xy", None, None),
        P("band"),
        P("band"),
        P("xy", None, None),
        P(None, "xy", None, None),
    )
    out_specs = (P(None, "xy", "band", None), P())
    return jax.shard_map(local, mesh=mesh, in_specs=in_specs, out_specs=out_specs, check_vma=False)
```

```python
import math

import jax
import jax.numpy as jnp
from jax import lax
from jax.sharding import PartitionSpec as P

ITERS = 3


def padded_2(block, sides, width):
    for axis, dim in sides:
        count = lax.axis_size(axis)
        forward = [(i, i + 1) for i in range(count - 1)]
        forward.append((count - 1, 0))
        backward = [(target, source) for source, target in forward]
        low = lax.ppermute(
            lax.slice_in_dim(block, block.shape[dim] - width, None, axis=dim), axis, forward
        )
        high = lax.ppermute(lax.slice_in_dim(block, 0, width, axis=dim), axis, backward)
        block = jnp.concatenate([low, block, high], axis=dim)
    return block


def tree_sum(value, axes):
    for axis in axes:
        count = lax.axis_size(axis)
        step = 1
        while step < count:
            pairs = [(i, i ^ step) for i in range(count)]
            value = value + lax.ppermute(value, axis, pairs)
            step *= 2
    return value


def tree_sum_parts(parts, axes):
    flat = jnp.concatenate([part.reshape(-1) for part in parts])
    flat = tree_sum(flat, axes)
    out, start = [], 0
    for part in parts:
        out.append(flat[start : start + part.size].reshape(part.shape))
        start += part.size
    return out


def neighbours_z(field_block):
    z_padded = jnp.pad(field_block, ((0, 0), (0, 0), (0, 0), (1, 1)))
    return z_padded[..., 2:] + z_padded[..., :-2]


def local(orbitals, energies, occupation, potential, trials):
    nb_dev, width_x, width_y, width_z = orbitals.shape
    trial_count = trials.shape[0]
    cell_count = width_x * width_y * width_z
    cell_total = cell_count * lax.axis_size("xy")
    orbital_total = nb_dev * lax.axis_size("band")
    row_count = nb_dev * trial_count
    highest = lax.Precision.HIGHEST

    def dot(a, b):
        return jnp.dot(a, b, precision=highest, preferred_element_type=jnp.float32)

    psi_flat = orbitals.reshape(nb_dev, cell_count)
    trial_flat = trials.reshape(trial_count, cell_count)
    psi_all = lax.all_gather(psi_flat, "band", axis=0, tiled=True)
    weight_rows = occupation.astype(jnp.float32)

    diagonal = 3.0 + potential.reshape(1, cell_count) - energies[:, None]
    diagonal_op = jnp.broadcast_to(
        diagonal[:, None, :], (nb_dev, trial_count, cell_count)
    ).reshape(row_count, cell_count)
    products = (psi_flat[:, None, :] * trial_flat[None, :, :]).reshape(row_count, cell_count)
    products_d = products / diagonal_op

    c0_part = dot(psi_all, products.T)
    cpd_part = dot(psi_all, products_d.T)
    scaled = (psi_all[None, :, :] / diagonal[:, None, :]).reshape(nb_dev * orbital_total, cell_count)
    gram_part = dot(scaled, psi_all.T).reshape(nb_dev, orbital_total, orbital_total)
    c0, cpd, gram = tree_sum_parts((c0_part, cpd_part, gram_part), ("xy",))
    c0 = c0 / cell_total
    cpd = cpd / cell_total
    gram = gram / cell_total

    right_side = dot(c0.T, psi_all) - products
    c0_rows = c0.reshape(orbital_total, nb_dev, trial_count)
    c1 = jnp.einsum("ijl,lik->jik", gram, c0_rows, precision=highest).reshape(
        orbital_total, row_count
    ) - cpd
    update = right_side / diagonal_op - dot(c1.T, psi_all)

    def apply_slab(vectors):
        field_block = vectors.reshape(-1, width_x, width_y, width_z)
        padded = padded_2(field_block, (("xy", 1),), 1)
        beside = padded[:, 2:] + padded[:, :-2]
        beside = beside + jnp.roll(field_block, 1, 2) + jnp.roll(field_block, -1, 2)
        beside = beside + neighbours_z(field_block)
        return diagonal_op * vectors - 0.5 * beside.reshape(vectors.shape)

    for iteration in range(ITERS):
        step = (right_side - apply_slab(update)) / diagonal_op
        if iteration < ITERS - 1:
            (inter,) = tree_sum_parts((dot(psi_all, step.T),), ("xy",))
            update = update + (step - dot((inter / cell_total).T, psi_all))
        else:
            pre = update + step
            pre_rows = pre.reshape(nb_dev, trial_count, cell_count)
            prod_rows = products.reshape(nb_dev, trial_count, cell_count)
            pair_part = jnp.einsum("ikc,ilc->ikl", pre_rows, prod_rows, precision=highest)
            inter, pair = tree_sum_parts((dot(psi_all, step.T), pair_part), ("xy",))
            inter = inter / cell_total
            pair = pair / cell_total
            update = update + (step - dot(inter.T, psi_all))

    inter_rows = inter.reshape(orbital_total, nb_dev, trial_count)
    cross = jnp.einsum("jik,jil->ikl", inter_rows, c0_rows, precision=highest)
    scale = weight_rows / math.sqrt(orbital_total)
    response_part = jnp.einsum("i,ikl->kl", scale, pair - cross, precision=highest)
    (response_matrix,) = tree_sum_parts((response_part,), ("band",))

    weights = weight_rows[:, None, None] * psi_flat[:, None, :]
    summed = jnp.sum(weights * update.reshape(nb_dev, trial_count, cell_count), axis=0)
    partial_grid = (summed / math.sqrt(orbital_total)).reshape(
        trial_count, width_x, width_y, width_z
    )
    density = lax.psum_scatter(partial_grid, "band", scatter_dimension=2, tiled=True)
    return (density, response_matrix)


def solution(mesh):
    in_specs = (
        P("band", "xy", None, None),
        P("band"),
        P("band"),
        P("xy", None, None),
        P(None, "xy", None, None),
    )
    out_specs = (P(None, "xy", "band", None), P())
    return jax.shard_map(local, mesh=mesh, in_specs=in_specs, out_specs=out_specs, check_vma=False)
```

```python
import math

import jax
import jax.numpy as jnp
from jax import lax
from jax.sharding import PartitionSpec as P

ITERS = 3


def padded_2(block, sides, width):
    for axis, dim in sides:
        count = lax.axis_size(axis)
        forward = [(i, i + 1) for i in range(count - 1)]
        forward.append((count - 1, 0))
        backward = [(target, source) for source, target in forward]
        low = lax.ppermute(
            lax.slice_in_dim(block, block.shape[dim] - width, None, axis=dim), axis, forward
        )
        high = lax.ppermute(lax.slice_in_dim(block, 0, width, axis=dim), axis, backward)
        block = jnp.concatenate([low, block, high], axis=dim)
    return block


def tree_sum(value, axes):
    for axis in axes:
        count = lax.axis_size(axis)
        step = 1
        while step < count:
            pairs = [(i, i ^ step) for i in range(count)]
            value = value + lax.ppermute(value, axis, pairs)
            step *= 2
    return value


def tree_sum_parts(parts, axes):
    flat = jnp.concatenate([part.reshape(-1) for part in parts])
    flat = tree_sum(flat, axes)
    out, start = [], 0
    for part in parts:
        out.append(flat[start : start + part.size].reshape(part.shape))
        start += part.size
    return out


def gather_rounds(block, axis):
    count = lax.axis_size(axis)
    step = 1
    while step < count:
        pairs = [(i, i ^ step) for i in range(count)]
        block = jnp.concatenate([block, lax.ppermute(block, axis, pairs)], axis=0)
        step *= 2
    return block


def scatter_rounds(grid, extra, axis, dim):
    count = lax.axis_size(axis)
    index = lax.axis_index(axis)
    step = count // 2
    while step >= 1:
        half = grid.shape[dim] // 2
        bit = (index // step) % 2
        kept = lax.dynamic_slice_in_dim(grid, bit * half, half, axis=dim)
        sent = lax.dynamic_slice_in_dim(grid, (1 - bit) * half, half, axis=dim)
        packed = jnp.concatenate([sent.reshape(-1), extra.reshape(-1)])
        pairs = [(i, i ^ step) for i in range(count)]
        received = lax.ppermute(packed, axis, pairs)
        grid = kept + received[: sent.size].reshape(sent.shape)
        extra = extra + received[sent.size :].reshape(extra.shape)
        step //= 2
    return grid, extra


def neighbours_z(field_block):
    z_padded = jnp.pad(field_block, ((0, 0), (0, 0), (0, 0), (1, 1)))
    return z_padded[..., 2:] + z_padded[..., :-2]


def local(orbitals, energies, occupation, potential, trials):
    nb_dev, width_x, width_y, width_z = orbitals.shape
    trial_count = trials.shape[0]
    cell_count = width_x * width_y * width_z
    cell_total = cell_count * lax.axis_size("xy")
    orbital_total = nb_dev * lax.axis_size("band")
    row_count = nb_dev * trial_count
    highest = lax.Precision.HIGHEST

    def dot(a, b):
        return jnp.dot(a, b, precision=highest, preferred_element_type=jnp.float32)

    psi_flat = orbitals.reshape(nb_dev, cell_count)
    trial_flat = trials.reshape(trial_count, cell_count)
    psi_all = gather_rounds(psi_flat, "band")
    weight_rows = occupation.astype(jnp.float32)

    diagonal = 3.0 + potential.reshape(1, cell_count) - energies[:, None]
    diagonal_op = jnp.broadcast_to(
        diagonal[:, None, :], (nb_dev, trial_count, cell_count)
    ).reshape(row_count, cell_count)
    products = (psi_flat[:, None, :] * trial_flat[None, :, :]).reshape(row_count, cell_count)
    products_d = products / diagonal_op

    c0_part = dot(psi_all, products.T)
    cpd_part = dot(psi_all, products_d.T)
    scaled = (psi_all[None, :, :] / diagonal[:, None, :]).reshape(nb_dev * orbital_total, cell_count)
    gram_part = dot(scaled, psi_all.T).reshape(nb_dev, orbital_total, orbital_total)
    c0, cpd, gram = tree_sum_parts((c0_part, cpd_part, gram_part), ("xy",))
    c0 = c0 / cell_total
    cpd = cpd / cell_total
    gram = gram / cell_total

    right_side = dot(c0.T, psi_all) - products
    c0_rows = c0.reshape(orbital_total, nb_dev, trial_count)
    c1 = jnp.einsum("ijl,lik->jik", gram, c0_rows, precision=highest).reshape(
        orbital_total, row_count
    ) - cpd
    update = right_side / diagonal_op - dot(c1.T, psi_all)

    def apply_slab(vectors):
        field_block = vectors.reshape(-1, width_x, width_y, width_z)
        padded = padded_2(field_block, (("xy", 1),), 1)
        beside = padded[:, 2:] + padded[:, :-2]
        beside = beside + jnp.roll(field_block, 1, 2) + jnp.roll(field_block, -1, 2)
        beside = beside + neighbours_z(field_block)
        return diagonal_op * vectors - 0.5 * beside.reshape(vectors.shape)

    for iteration in range(ITERS):
        step = (right_side - apply_slab(update)) / diagonal_op
        if iteration < ITERS - 1:
            (inter,) = tree_sum_parts((dot(psi_all, step.T),), ("xy",))
            update = update + (step - dot((inter / cell_total).T, psi_all))
        else:
            pre = update + step
            pre_rows = pre.reshape(nb_dev, trial_count, cell_count)
            prod_rows = products.reshape(nb_dev, trial_count, cell_count)
            pair_part = jnp.einsum("ikc,ilc->ikl", pre_rows, prod_rows, precision=highest)
            inter, pair = tree_sum_parts((dot(psi_all, step.T), pair_part), ("xy",))
            inter = inter / cell_total
            pair = pair / cell_total
            update = update + (step - dot(inter.T, psi_all))

    inter_rows = inter.reshape(orbital_total, nb_dev, trial_count)
    cross = jnp.einsum("jik,jil->ikl", inter_rows, c0_rows, precision=highest)
    scale = weight_rows / math.sqrt(orbital_total)
    response_part = jnp.einsum("i,ikl->kl", scale, pair - cross, precision=highest)

    weights = weight_rows[:, None, None] * psi_flat[:, None, :]
    summed = jnp.sum(weights * update.reshape(nb_dev, trial_count, cell_count), axis=0)
    partial_grid = (summed / math.sqrt(orbital_total)).reshape(
        trial_count, width_x, width_y, width_z
    )
    density, response_matrix = scatter_rounds(partial_grid, response_part, "band", 2)
    return (density, response_matrix)


def solution(mesh):
    in_specs = (
        P("band", "xy", None, None),
        P("band"),
        P("band"),
        P("xy", None, None),
        P(None, "xy", None, None),
    )
    out_specs = (P(None, "xy", "band", None), P())
    return jax.shard_map(local, mesh=mesh, in_specs=in_specs, out_specs=out_specs, check_vma=False)
```

```python
import math

import jax
import jax.numpy as jnp
from jax import lax
from jax.sharding import PartitionSpec as P


ITERS = 3


def padded_2(block, sides, width):
    for axis, dim in sides:
        count = lax.axis_size(axis)
        forward = [(i, i + 1) for i in range(count - 1)]
        forward.append((count - 1, 0))
        backward = [(target, source) for source, target in forward]
        low = lax.ppermute(
            lax.slice_in_dim(block, block.shape[dim] - width, None, axis=dim), axis, forward
        )
        high = lax.ppermute(lax.slice_in_dim(block, 0, width, axis=dim), axis, backward)
        block = jnp.concatenate([low, block, high], axis=dim)
    return block


def tree_sum(value, axes):
    for axis in axes:
        count = lax.axis_size(axis)
        step = 1
        while step < count:
            pairs = [(i, i ^ step) for i in range(count)]
            value = value + lax.ppermute(value, axis, pairs)
            step *= 2
    return value


def tree_sum_parts(parts, axes):
    flat = jnp.concatenate([part.reshape(-1) for part in parts])
    flat = tree_sum(flat, axes)
    out, start = [], 0
    for part in parts:
        out.append(flat[start : start + part.size].reshape(part.shape))
        start += part.size
    return out


def gather_rounds(block, axis):
    count = lax.axis_size(axis)
    step = 1
    while step < count:
        pairs = [(i, i ^ step) for i in range(count)]
        block = jnp.concatenate([block, lax.ppermute(block, axis, pairs)], axis=0)
        step *= 2
    return block


def scatter_rounds(grid, extra, axis, dim):
    count = lax.axis_size(axis)
    index = lax.axis_index(axis)
    step = count // 2
    while step >= 1:
        half = grid.shape[dim] // 2
        bit = (index // step) % 2
        kept = lax.dynamic_slice_in_dim(grid, bit * half, half, axis=dim)
        sent = lax.dynamic_slice_in_dim(grid, (1 - bit) * half, half, axis=dim)
        packed = jnp.concatenate([sent.reshape(-1), extra.reshape(-1)])
        pairs = [(i, i ^ step) for i in range(count)]
        received = lax.ppermute(packed, axis, pairs)
        grid = kept + received[: sent.size].reshape(sent.shape)
        extra = extra + received[sent.size :].reshape(extra.shape)
        step //= 2
    return grid, extra


def neighbours_z(field_block):
    z_padded = jnp.pad(field_block, ((0, 0), (0, 0), (0, 0), (1, 1)))
    return z_padded[..., 2:] + z_padded[..., :-2]


def local(orbitals, energies, occupation, potential, trials):
    nb_dev, width_x, width_y, width_z = orbitals.shape
    trial_count = trials.shape[0]
    cell_count = width_x * width_y * width_z
    cell_total = cell_count * lax.axis_size("xy")
    orbital_total = nb_dev * lax.axis_size("band")
    row_count = nb_dev * trial_count
    highest = lax.Precision.HIGHEST

    def dot(a, b):
        return jnp.dot(a, b, precision=highest, preferred_element_type=jnp.float32)

    psi_flat = orbitals.reshape(nb_dev, cell_count)
    trial_flat = trials.reshape(trial_count, cell_count)
    psi_all = gather_rounds(psi_flat, "band")
    weight_rows = occupation.astype(jnp.float32)

    diagonal = 3.0 + potential.reshape(1, cell_count) - energies[:, None]
    diagonal_op = jnp.broadcast_to(
        diagonal[:, None, :], (nb_dev, trial_count, cell_count)
    ).reshape(row_count, cell_count)
    products = (psi_flat[:, None, :] * trial_flat[None, :, :]).reshape(row_count, cell_count)
    products_d = products / diagonal_op

    c0_part = dot(psi_all, products.T)
    cpd_part = dot(psi_all, products_d.T)
    scaled = (psi_all[None, :, :] / diagonal[:, None, :]).reshape(nb_dev * orbital_total, cell_count)
    gram_part = dot(scaled, psi_all.T).reshape(nb_dev, orbital_total, orbital_total)
    c0, cpd, gram = tree_sum_parts((c0_part, cpd_part, gram_part), ("xy",))
    c0 = c0 / cell_total
    cpd = cpd / cell_total
    gram = gram / cell_total

    right_side = dot(c0.T, psi_all) - products
    c0_rows = c0.reshape(orbital_total, nb_dev, trial_count)
    c1 = jnp.einsum("ijl,lik->jik", gram, c0_rows, precision=highest).reshape(
        orbital_total, row_count
    ) - cpd
    update = right_side / diagonal_op - dot(c1.T, psi_all)

    def beside_x(vectors):
        field_block = vectors.reshape(-1, width_x, width_y, width_z)
        padded = padded_2(field_block, (("xy", 1),), 1)
        return (padded[:, 2:] + padded[:, :-2]).reshape(vectors.shape)

    def apply_slab(vectors, beside_planes):
        field_block = vectors.reshape(-1, width_x, width_y, width_z)
        beside = beside_planes.reshape(field_block.shape)
        beside = beside + jnp.roll(field_block, 1, 2) + jnp.roll(field_block, -1, 2)
        beside = beside + neighbours_z(field_block)
        return diagonal_op * vectors - 0.5 * beside.reshape(vectors.shape)

    psi_beside = beside_x(psi_all)
    update_beside = beside_x(update)
    for iteration in range(ITERS):
        step = (right_side - apply_slab(update, update_beside)) / diagonal_op
        if iteration < ITERS - 1:
            pre_beside = beside_x(update + step)
            (inter,) = tree_sum_parts((dot(psi_all, step.T),), ("xy",))
            inter = inter / cell_total
            update = update + (step - dot(inter.T, psi_all))
            update_beside = pre_beside - dot(inter.T, psi_beside)
        else:
            pre = update + step
            pre_rows = pre.reshape(nb_dev, trial_count, cell_count)
            prod_rows = products.reshape(nb_dev, trial_count, cell_count)
            pair_part = jnp.einsum("ikc,ilc->ikl", pre_rows, prod_rows, precision=highest)
            inter, pair = tree_sum_parts((dot(psi_all, step.T), pair_part), ("xy",))
            inter = inter / cell_total
            pair = pair / cell_total
            update = update + (step - dot(inter.T, psi_all))

    inter_rows = inter.reshape(orbital_total, nb_dev, trial_count)
    cross = jnp.einsum("jik,jil->ikl", inter_rows, c0_rows, precision=highest)
    scale = weight_rows / math.sqrt(orbital_total)
    response_part = jnp.einsum("i,ikl->kl", scale, pair - cross, precision=highest)

    weights = weight_rows[:, None, None] * psi_flat[:, None, :]
    summed = jnp.sum(weights * update.reshape(nb_dev, trial_count, cell_count), axis=0)
    partial_grid = (summed / math.sqrt(orbital_total)).reshape(
        trial_count, width_x, width_y, width_z
    )
    density, response_matrix = scatter_rounds(partial_grid, response_part, "band", 2)
    return (density, response_matrix)


def solution(mesh):
    in_specs = (
        P("band", "xy", None, None),
        P("band"),
        P("band"),
        P("xy", None, None),
        P(None, "xy", None, None),
    )
    out_specs = (P(None, "xy", "band", None), P())
    return jax.shard_map(local, mesh=mesh, in_specs=in_specs, out_specs=out_specs, check_vma=False)
```

```python
import math

import jax
import jax.numpy as jnp
from jax import lax
from jax.sharding import PartitionSpec as P


ITERS = 3


def padded_2(block, sides, width):
    for axis, dim in sides:
        count = lax.axis_size(axis)
        forward = [(i, i + 1) for i in range(count - 1)]
        forward.append((count - 1, 0))
        backward = [(target, source) for source, target in forward]
        low = lax.ppermute(
            lax.slice_in_dim(block, block.shape[dim] - width, None, axis=dim), axis, forward
        )
        high = lax.ppermute(lax.slice_in_dim(block, 0, width, axis=dim), axis, backward)
        block = jnp.concatenate([low, block, high], axis=dim)
    return block


def tree_sum(value, axes):
    for axis in axes:
        count = lax.axis_size(axis)
        step = 1
        while step < count:
            pairs = [(i, i ^ step) for i in range(count)]
            value = value + lax.ppermute(value, axis, pairs)
            step *= 2
    return value


def tree_sum_parts(parts, axes):
    flat = jnp.concatenate([part.reshape(-1) for part in parts])
    flat = tree_sum(flat, axes)
    out, start = [], 0
    for part in parts:
        out.append(flat[start : start + part.size].reshape(part.shape))
        start += part.size
    return out


def scatter_rounds(grid, extra, axis, dim):
    count = lax.axis_size(axis)
    index = lax.axis_index(axis)
    step = count // 2
    while step >= 1:
        half = grid.shape[dim] // 2
        bit = (index // step) % 2
        kept = lax.dynamic_slice_in_dim(grid, bit * half, half, axis=dim)
        sent = lax.dynamic_slice_in_dim(grid, (1 - bit) * half, half, axis=dim)
        packed = jnp.concatenate([sent.reshape(-1), extra.reshape(-1)])
        pairs = [(i, i ^ step) for i in range(count)]
        received = lax.ppermute(packed, axis, pairs)
        grid = kept + received[: sent.size].reshape(sent.shape)
        extra = extra + received[sent.size :].reshape(extra.shape)
        step //= 2
    return grid, extra


def neighbours_z(field_block):
    z_padded = jnp.pad(field_block, ((0, 0), (0, 0), (0, 0), (1, 1)))
    return z_padded[..., 2:] + z_padded[..., :-2]


def local(orbitals, energies, occupation, potential, trials):
    nb_dev, width_x, width_y, width_z = orbitals.shape
    trial_count = trials.shape[0]
    cell_count = width_x * width_y * width_z
    cell_total = cell_count * lax.axis_size("xy")
    orbital_total = nb_dev * lax.axis_size("band")
    row_count = nb_dev * trial_count
    highest = lax.Precision.HIGHEST

    def dot(a, b):
        return jnp.dot(a, b, precision=highest, preferred_element_type=jnp.float32)

    psi_flat = orbitals.reshape(nb_dev, cell_count)
    trial_flat = trials.reshape(trial_count, cell_count)
    psi_all = lax.all_gather(psi_flat, "band", axis=0, tiled=True)
    weight_rows = occupation.astype(jnp.float32)

    diagonal = 3.0 + potential.reshape(1, cell_count) - energies[:, None]
    diagonal_op = jnp.broadcast_to(
        diagonal[:, None, :], (nb_dev, trial_count, cell_count)
    ).reshape(row_count, cell_count)
    products = (psi_flat[:, None, :] * trial_flat[None, :, :]).reshape(row_count, cell_count)
    products_d = products / diagonal_op

    c0_part = dot(psi_all, products.T)
    cpd_part = dot(psi_all, products_d.T)
    scaled = (psi_all[None, :, :] / diagonal[:, None, :]).reshape(nb_dev * orbital_total, cell_count)
    gram_part = dot(scaled, psi_all.T).reshape(nb_dev, orbital_total, orbital_total)
    c0, cpd, gram = tree_sum_parts((c0_part, cpd_part, gram_part), ("xy",))
    c0 = c0 / cell_total
    cpd = cpd / cell_total
    gram = gram / cell_total

    right_side = dot(c0.T, psi_all) - products
    c0_rows = c0.reshape(orbital_total, nb_dev, trial_count)
    c1 = jnp.einsum("ijl,lik->jik", gram, c0_rows, precision=highest).reshape(
        orbital_total, row_count
    ) - cpd
    update = right_side / diagonal_op - dot(c1.T, psi_all)

    def beside_x(vectors):
        field_block = vectors.reshape(-1, width_x, width_y, width_z)
        padded = padded_2(field_block, (("xy", 1),), 1)
        return (padded[:, 2:] + padded[:, :-2]).reshape(vectors.shape)

    def apply_slab(vectors, beside_planes):
        field_block = vectors.reshape(-1, width_x, width_y, width_z)
        beside = beside_planes.reshape(field_block.shape)
        beside = beside + jnp.roll(field_block, 1, 2) + jnp.roll(field_block, -1, 2)
        beside = beside + neighbours_z(field_block)
        return diagonal_op * vectors - 0.5 * beside.reshape(vectors.shape)

    psi_beside = lax.all_gather(beside_x(psi_flat), "band", axis=0, tiled=True)
    update_beside = beside_x(update)
    for iteration in range(ITERS):
        step = (right_side - apply_slab(update, update_beside)) / diagonal_op
        if iteration < ITERS - 1:
            pre_beside = beside_x(update + step)
            (inter,) = tree_sum_parts((dot(psi_all, step.T),), ("xy",))
            inter = inter / cell_total
            update = update + (step - dot(inter.T, psi_all))
            update_beside = pre_beside - dot(inter.T, psi_beside)
        else:
            pre = update + step
            pre_rows = pre.reshape(nb_dev, trial_count, cell_count)
            prod_rows = products.reshape(nb_dev, trial_count, cell_count)
            pair_part = jnp.einsum("ikc,ilc->ikl", pre_rows, prod_rows, precision=highest)
            inter, pair = tree_sum_parts((dot(psi_all, step.T), pair_part), ("xy",))
            inter = inter / cell_total
            pair = pair / cell_total
            update = update + (step - dot(inter.T, psi_all))

    inter_rows = inter.reshape(orbital_total, nb_dev, trial_count)
    cross = jnp.einsum("jik,jil->ikl", inter_rows, c0_rows, precision=highest)
    scale = weight_rows / math.sqrt(orbital_total)
    response_part = jnp.einsum("i,ikl->kl", scale, pair - cross, precision=highest)

    weights = weight_rows[:, None, None] * psi_flat[:, None, :]
    summed = jnp.sum(weights * update.reshape(nb_dev, trial_count, cell_count), axis=0)
    partial_grid = (summed / math.sqrt(orbital_total)).reshape(
        trial_count, width_x, width_y, width_z
    )
    density, response_matrix = scatter_rounds(partial_grid, response_part, "band", 2)
    return (density, response_matrix)


def solution(mesh):
    in_specs = (
        P("band", "xy", None, None),
        P("band"),
        P("band"),
        P("xy", None, None),
        P(None, "xy", None, None),
    )
    out_specs = (P(None, "xy", "band", None), P())
    return jax.shard_map(local, mesh=mesh, in_specs=in_specs, out_specs=out_specs, check_vma=False)
```

```python
import math

import jax
import jax.numpy as jnp
from jax import lax
from jax.sharding import PartitionSpec as P

ITERS = 3


def padded_2(block, sides, width):
    for axis, dim in sides:
        count = lax.axis_size(axis)
        forward = [(i, i + 1) for i in range(count - 1)]
        forward.append((count - 1, 0))
        backward = [(target, source) for source, target in forward]
        low = lax.ppermute(
            lax.slice_in_dim(block, block.shape[dim] - width, None, axis=dim), axis, forward
        )
        high = lax.ppermute(lax.slice_in_dim(block, 0, width, axis=dim), axis, backward)
        block = jnp.concatenate([low, block, high], axis=dim)
    return block


def tree_sum(value, axes):
    for axis in axes:
        count = lax.axis_size(axis)
        step = 1
        while step < count:
            pairs = [(i, i ^ step) for i in range(count)]
            value = value + lax.ppermute(value, axis, pairs)
            step *= 2
    return value


def tree_sum_parts(parts, axes):
    flat = jnp.concatenate([part.reshape(-1) for part in parts])
    flat = tree_sum(flat, axes)
    out, start = [], 0
    for part in parts:
        out.append(flat[start : start + part.size].reshape(part.shape))
        start += part.size
    return out


def scatter_rounds(grid, extra, axis, dim):
    count = lax.axis_size(axis)
    index = lax.axis_index(axis)
    step = count // 2
    while step >= 1:
        half = grid.shape[dim] // 2
        bit = (index // step) % 2
        kept = lax.dynamic_slice_in_dim(grid, bit * half, half, axis=dim)
        sent = lax.dynamic_slice_in_dim(grid, (1 - bit) * half, half, axis=dim)
        packed = jnp.concatenate([sent.reshape(-1), extra.reshape(-1)])
        pairs = [(i, i ^ step) for i in range(count)]
        received = lax.ppermute(packed, axis, pairs)
        grid = kept + received[: sent.size].reshape(sent.shape)
        extra = extra + received[sent.size :].reshape(extra.shape)
        step //= 2
    return grid, extra


def neighbours_z(field_block):
    z_padded = jnp.pad(field_block, ((0, 0), (0, 0), (0, 0), (1, 1)))
    return z_padded[..., 2:] + z_padded[..., :-2]


def local(orbitals, energies, occupation, potential, trials):
    nb_dev, width_x, width_y, width_z = orbitals.shape
    trial_count = trials.shape[0]
    cell_count = width_x * width_y * width_z
    cell_total = cell_count * lax.axis_size("xy")
    orbital_total = nb_dev * lax.axis_size("band")
    row_count = nb_dev * trial_count
    highest = lax.Precision.HIGHEST

    def dot(a, b):
        return jnp.dot(a, b, precision=highest, preferred_element_type=jnp.float32)

    psi_flat = orbitals.reshape(nb_dev, cell_count)
    trial_flat = trials.reshape(trial_count, cell_count)
    psi_all = lax.all_gather(psi_flat, "band", axis=0, tiled=True)
    weight_rows = occupation.astype(jnp.float32)

    diagonal = 3.0 + potential.reshape(1, cell_count) - energies[:, None]
    diagonal_op = jnp.broadcast_to(
        diagonal[:, None, :], (nb_dev, trial_count, cell_count)
    ).reshape(row_count, cell_count)
    products = (psi_flat[:, None, :] * trial_flat[None, :, :]).reshape(row_count, cell_count)
    products_d = products / diagonal_op

    c0_part = dot(psi_all, products.T)
    cpd_part = dot(psi_all, products_d.T)
    scaled = (psi_all[None, :, :] / diagonal[:, None, :]).reshape(nb_dev * orbital_total, cell_count)
    gram_part = dot(scaled, psi_all.T).reshape(nb_dev, orbital_total, orbital_total)
    c0, cpd, gram = tree_sum_parts((c0_part, cpd_part, gram_part), ("xy",))
    c0 = c0 / cell_total
    cpd = cpd / cell_total
    gram = gram / cell_total

    right_side = dot(c0.T, psi_all) - products
    c0_rows = c0.reshape(orbital_total, nb_dev, trial_count)
    c1 = jnp.einsum("ijl,lik->jik", gram, c0_rows, precision=highest).reshape(
        orbital_total, row_count
    ) - cpd
    update = right_side / diagonal_op - dot(c1.T, psi_all)

    def apply_slab(vectors):
        field_block = vectors.reshape(-1, width_x, width_y, width_z)
        padded = padded_2(field_block, (("xy", 1),), 1)
        beside = padded[:, 2:] + padded[:, :-2]
        beside = beside + jnp.roll(field_block, 1, 2) + jnp.roll(field_block, -1, 2)
        beside = beside + neighbours_z(field_block)
        return diagonal_op * vectors - 0.5 * beside.reshape(vectors.shape)

    for iteration in range(ITERS):
        step = (right_side - apply_slab(update)) / diagonal_op
        if iteration < ITERS - 1:
            (inter,) = tree_sum_parts((dot(psi_all, step.T),), ("xy",))
            update = update + (step - dot((inter / cell_total).T, psi_all))
        else:
            pre = update + step
            pre_rows = pre.reshape(nb_dev, trial_count, cell_count)
            prod_rows = products.reshape(nb_dev, trial_count, cell_count)
            pair_part = jnp.einsum("ikc,ilc->ikl", pre_rows, prod_rows, precision=highest)
            inter, pair = tree_sum_parts((dot(psi_all, step.T), pair_part), ("xy",))
            inter = inter / cell_total
            pair = pair / cell_total
            update = update + (step - dot(inter.T, psi_all))

    inter_rows = inter.reshape(orbital_total, nb_dev, trial_count)
    cross = jnp.einsum("jik,jil->ikl", inter_rows, c0_rows, precision=highest)
    scale = weight_rows / math.sqrt(orbital_total)
    response_part = jnp.einsum("i,ikl->kl", scale, pair - cross, precision=highest)

    weights = weight_rows[:, None, None] * psi_flat[:, None, :]
    summed = jnp.sum(weights * update.reshape(nb_dev, trial_count, cell_count), axis=0)
    partial_grid = (summed / math.sqrt(orbital_total)).reshape(
        trial_count, width_x, width_y, width_z
    )
    density, response_matrix = scatter_rounds(partial_grid, response_part, "band", 2)
    return (density, response_matrix)


def solution(mesh):
    in_specs = (
        P("band", "xy", None, None),
        P("band"),
        P("band"),
        P("xy", None, None),
        P(None, "xy", None, None),
    )
    out_specs = (P(None, "xy", "band", None), P())
    return jax.shard_map(local, mesh=mesh, in_specs=in_specs, out_specs=out_specs, check_vma=False)
```

```python
import math

import jax
import jax.numpy as jnp
from jax import lax
from jax.sharding import PartitionSpec as P

ITERS = 3


def padded_2(block, sides, width):
    for axis, dim in sides:
        count = lax.axis_size(axis)
        forward = [(i, i + 1) for i in range(count - 1)]
        forward.append((count - 1, 0))
        backward = [(target, source) for source, target in forward]
        low = lax.ppermute(
            lax.slice_in_dim(block, block.shape[dim] - width, None, axis=dim), axis, forward
        )
        high = lax.ppermute(lax.slice_in_dim(block, 0, width, axis=dim), axis, backward)
        block = jnp.concatenate([low, block, high], axis=dim)
    return block


def tree_sum(value, axes):
    for axis in axes:
        count = lax.axis_size(axis)
        step = 1
        while step < count:
            pairs = [(i, i ^ step) for i in range(count)]
            value = value + lax.ppermute(value, axis, pairs)
            step *= 2
    return value


def tree_sum_parts(parts, axes):
    flat = jnp.concatenate([part.reshape(-1) for part in parts])
    flat = tree_sum(flat, axes)
    out, start = [], 0
    for part in parts:
        out.append(flat[start : start + part.size].reshape(part.shape))
        start += part.size
    return out


def gather_rounds(block, axis):
    count = lax.axis_size(axis)
    step = 1
    while step < count:
        pairs = [(i, i ^ step) for i in range(count)]
        block = jnp.concatenate([block, lax.ppermute(block, axis, pairs)], axis=0)
        step *= 2
    return block


def scatter_rounds(grid, extra, axis, dim):
    count = lax.axis_size(axis)
    index = lax.axis_index(axis)
    step = count // 2
    while step >= 1:
        half = grid.shape[dim] // 2
        bit = (index // step) % 2
        kept = lax.dynamic_slice_in_dim(grid, bit * half, half, axis=dim)
        sent = lax.dynamic_slice_in_dim(grid, (1 - bit) * half, half, axis=dim)
        packed = jnp.concatenate([sent.reshape(-1), extra.reshape(-1)])
        pairs = [(i, i ^ step) for i in range(count)]
        received = lax.ppermute(packed, axis, pairs)
        grid = kept + received[: sent.size].reshape(sent.shape)
        extra = extra + received[sent.size :].reshape(extra.shape)
        step //= 2
    return grid, extra


def neighbours_z(field_block):
    z_padded = jnp.pad(field_block, ((0, 0), (0, 0), (0, 0), (1, 1)))
    return z_padded[..., 2:] + z_padded[..., :-2]


def local(orbitals, energies, occupation, potential, trials):
    nb_dev, width_x, width_y, width_z = orbitals.shape
    trial_count = trials.shape[0]
    cell_count = width_x * width_y * width_z
    cell_total = cell_count * lax.axis_size("xy")
    orbital_total = nb_dev * lax.axis_size("band")
    row_count = nb_dev * trial_count
    highest = lax.Precision.HIGHEST

    def dot(a, b):
        return jnp.dot(a, b, precision=highest, preferred_element_type=jnp.float32)

    psi_flat = orbitals.reshape(nb_dev, cell_count)
    trial_flat = trials.reshape(trial_count, cell_count)
    half = cell_count // 2
    band_count = lax.axis_size("band")
    psi_low = gather_rounds(psi_flat[:, :half], "band")
    psi_high = lax.all_gather(psi_flat[:, half:], "band", axis=0)
    order = jnp.bitwise_xor(lax.axis_index("band"), jnp.arange(band_count, dtype=jnp.int32))
    psi_high = jnp.take(psi_high, order, axis=0).reshape(orbital_total, cell_count - half)
    psi_all = jnp.concatenate([psi_low, psi_high], axis=1)
    weight_rows = occupation.astype(jnp.float32)

    diagonal = 3.0 + potential.reshape(1, cell_count) - energies[:, None]
    diagonal_op = jnp.broadcast_to(
        diagonal[:, None, :], (nb_dev, trial_count, cell_count)
    ).reshape(row_count, cell_count)
    products = (psi_flat[:, None, :] * trial_flat[None, :, :]).reshape(row_count, cell_count)
    products_d = products / diagonal_op

    c0_part = dot(psi_all, products.T)
    cpd_part = dot(psi_all, products_d.T)
    scaled = (psi_all[None, :, :] / diagonal[:, None, :]).reshape(nb_dev * orbital_total, cell_count)
    gram_part = dot(scaled, psi_all.T).reshape(nb_dev, orbital_total, orbital_total)
    c0, cpd, gram = tree_sum_parts((c0_part, cpd_part, gram_part), ("xy",))
    c0 = c0 / cell_total
    cpd = cpd / cell_total
    gram = gram / cell_total

    right_side = dot(c0.T, psi_all) - products
    c0_rows = c0.reshape(orbital_total, nb_dev, trial_count)
    c1 = jnp.einsum("ijl,lik->jik", gram, c0_rows, precision=highest).reshape(
        orbital_total, row_count
    ) - cpd
    update = right_side / diagonal_op - dot(c1.T, psi_all)

    def apply_slab(vectors):
        field_block = vectors.reshape(-1, width_x, width_y, width_z)
        padded = padded_2(field_block, (("xy", 1),), 1)
        beside = padded[:, 2:] + padded[:, :-2]
        beside = beside + jnp.roll(field_block, 1, 2) + jnp.roll(field_block, -1, 2)
        beside = beside + neighbours_z(field_block)
        return diagonal_op * vectors - 0.5 * beside.reshape(vectors.shape)

    for iteration in range(ITERS):
        step = (right_side - apply_slab(update)) / diagonal_op
        if iteration < ITERS - 1:
            (inter,) = tree_sum_parts((dot(psi_all, step.T),), ("xy",))
            update = update + (step - dot((inter / cell_total).T, psi_all))
        else:
            pre = update + step
            pre_rows = pre.reshape(nb_dev, trial_count, cell_count)
            prod_rows = products.reshape(nb_dev, trial_count, cell_count)
            pair_part = jnp.einsum("ikc,ilc->ikl", pre_rows, prod_rows, precision=highest)
            inter, pair = tree_sum_parts((dot(psi_all, step.T), pair_part), ("xy",))
            inter = inter / cell_total
            pair = pair / cell_total
            update = update + (step - dot(inter.T, psi_all))

    inter_rows = inter.reshape(orbital_total, nb_dev, trial_count)
    cross = jnp.einsum("jik,jil->ikl", inter_rows, c0_rows, precision=highest)
    scale = weight_rows / math.sqrt(orbital_total)
    response_part = jnp.einsum("i,ikl->kl", scale, pair - cross, precision=highest)

    weights = weight_rows[:, None, None] * psi_flat[:, None, :]
    summed = jnp.sum(weights * update.reshape(nb_dev, trial_count, cell_count), axis=0)
    partial_grid = (summed / math.sqrt(orbital_total)).reshape(
        trial_count, width_x, width_y, width_z
    )
    density, response_matrix = scatter_rounds(partial_grid, response_part, "band", 2)
    return (density, response_matrix)


def solution(mesh):
    in_specs = (
        P("band", "xy", None, None),
        P("band"),
        P("band"),
        P("xy", None, None),
        P(None, "xy", None, None),
    )
    out_specs = (P(None, "xy", "band", None), P())
    return jax.shard_map(local, mesh=mesh, in_specs=in_specs, out_specs=out_specs, check_vma=False)
```

```python
import math

import jax
import jax.numpy as jnp
from jax import lax
from jax.sharding import PartitionSpec as P

ITERS = 3


def padded_2(block, sides, width):
    for axis, dim in sides:
        count = lax.axis_size(axis)
        forward = [(i, i + 1) for i in range(count - 1)]
        forward.append((count - 1, 0))
        backward = [(target, source) for source, target in forward]
        low = lax.ppermute(
            lax.slice_in_dim(block, block.shape[dim] - width, None, axis=dim), axis, forward
        )
        high = lax.ppermute(lax.slice_in_dim(block, 0, width, axis=dim), axis, backward)
        block = jnp.concatenate([low, block, high], axis=dim)
    return block


def tree_sum(value, axes):
    for axis in axes:
        count = lax.axis_size(axis)
        step = 1
        while step < count:
            pairs = [(i, i ^ step) for i in range(count)]
            value = value + lax.ppermute(value, axis, pairs)
            step *= 2
    return value


def tree_sum_parts(parts, axes):
    flat = jnp.concatenate([part.reshape(-1) for part in parts])
    flat = tree_sum(flat, axes)
    out, start = [], 0
    for part in parts:
        out.append(flat[start : start + part.size].reshape(part.shape))
        start += part.size
    return out


def gather_rounds(block, axis):
    count = lax.axis_size(axis)
    step = count // 2
    while step >= 1:
        pairs = [(i, i ^ step) for i in range(count)]
        block = jnp.concatenate([block, lax.ppermute(block, axis, pairs)], axis=0)
        step //= 2
    return block


def scatter_rounds(grid, extra, axis, dim):
    count = lax.axis_size(axis)
    index = lax.axis_index(axis)
    step = count // 2
    while step >= 1:
        half = grid.shape[dim] // 2
        bit = (index // step) % 2
        kept = lax.dynamic_slice_in_dim(grid, bit * half, half, axis=dim)
        sent = lax.dynamic_slice_in_dim(grid, (1 - bit) * half, half, axis=dim)
        packed = jnp.concatenate([sent.reshape(-1), extra.reshape(-1)])
        pairs = [(i, i ^ step) for i in range(count)]
        received = lax.ppermute(packed, axis, pairs)
        grid = kept + received[: sent.size].reshape(sent.shape)
        extra = extra + received[sent.size :].reshape(extra.shape)
        step //= 2
    return grid, extra


def neighbours_z(field_block):
    z_padded = jnp.pad(field_block, ((0, 0), (0, 0), (0, 0), (1, 1)))
    return z_padded[..., 2:] + z_padded[..., :-2]


def local(orbitals, energies, occupation, potential, trials):
    nb_dev, width_x, width_y, width_z = orbitals.shape
    trial_count = trials.shape[0]
    cell_count = width_x * width_y * width_z
    cell_total = cell_count * lax.axis_size("xy")
    orbital_total = nb_dev * lax.axis_size("band")
    row_count = nb_dev * trial_count
    highest = lax.Precision.HIGHEST

    def dot(a, b):
        return jnp.dot(a, b, precision=highest, preferred_element_type=jnp.float32)

    psi_flat = orbitals.reshape(nb_dev, cell_count)
    trial_flat = trials.reshape(trial_count, cell_count)
    psi_all = gather_rounds(psi_flat, "band")
    weight_rows = occupation.astype(jnp.float32)

    diagonal = 3.0 + potential.reshape(1, cell_count) - energies[:, None]
    diagonal_op = jnp.broadcast_to(
        diagonal[:, None, :], (nb_dev, trial_count, cell_count)
    ).reshape(row_count, cell_count)
    products = (psi_flat[:, None, :] * trial_flat[None, :, :]).reshape(row_count, cell_count)
    products_d = products / diagonal_op

    c0_part = dot(psi_all, products.T)
    cpd_part = dot(psi_all, products_d.T)
    scaled = (psi_all[None, :, :] / diagonal[:, None, :]).reshape(nb_dev * orbital_total, cell_count)
    gram_part = dot(scaled, psi_all.T).reshape(nb_dev, orbital_total, orbital_total)
    c0, cpd, gram = tree_sum_parts((c0_part, cpd_part, gram_part), ("xy",))
    c0 = c0 / cell_total
    cpd = cpd / cell_total
    gram = gram / cell_total

    right_side = dot(c0.T, psi_all) - products
    c0_rows = c0.reshape(orbital_total, nb_dev, trial_count)
    c1 = jnp.einsum("ijl,lik->jik", gram, c0_rows, precision=highest).reshape(
        orbital_total, row_count
    ) - cpd
    update = right_side / diagonal_op - dot(c1.T, psi_all)

    def apply_slab(vectors):
        field_block = vectors.reshape(-1, width_x, width_y, width_z)
        padded = padded_2(field_block, (("xy", 1),), 1)
        beside = padded[:, 2:] + padded[:, :-2]
        beside = beside + jnp.roll(field_block, 1, 2) + jnp.roll(field_block, -1, 2)
        beside = beside + neighbours_z(field_block)
        return diagonal_op * vectors - 0.5 * beside.reshape(vectors.shape)

    for iteration in range(ITERS):
        step = (right_side - apply_slab(update)) / diagonal_op
        if iteration < ITERS - 1:
            (inter,) = tree_sum_parts((dot(psi_all, step.T),), ("xy",))
            update = update + (step - dot((inter / cell_total).T, psi_all))
        else:
            pre = update + step
            pre_rows = pre.reshape(nb_dev, trial_count, cell_count)
            prod_rows = products.reshape(nb_dev, trial_count, cell_count)
            pair_part = jnp.einsum("ikc,ilc->ikl", pre_rows, prod_rows, precision=highest)
            inter, pair = tree_sum_parts((dot(psi_all, step.T), pair_part), ("xy",))
            inter = inter / cell_total
            pair = pair / cell_total
            update = update + (step - dot(inter.T, psi_all))

    inter_rows = inter.reshape(orbital_total, nb_dev, trial_count)
    cross = jnp.einsum("jik,jil->ikl", inter_rows, c0_rows, precision=highest)
    scale = weight_rows / math.sqrt(orbital_total)
    response_part = jnp.einsum("i,ikl->kl", scale, pair - cross, precision=highest)

    weights = weight_rows[:, None, None] * psi_flat[:, None, :]
    summed = jnp.sum(weights * update.reshape(nb_dev, trial_count, cell_count), axis=0)
    partial_grid = (summed / math.sqrt(orbital_total)).reshape(
        trial_count, width_x, width_y, width_z
    )
    density, response_matrix = scatter_rounds(partial_grid, response_part, "band", 2)
    return (density, response_matrix)


def solution(mesh):
    in_specs = (
        P("band", "xy", None, None),
        P("band"),
        P("band"),
        P("xy", None, None),
        P(None, "xy", None, None),
    )
    out_specs = (P(None, "xy", "band", None), P())
    return jax.shard_map(local, mesh=mesh, in_specs=in_specs, out_specs=out_specs, check_vma=False)
```
